512 devices in a mesh: dp: 8 (over y_hi, x), expert: 64 (over y_lo, z, core).
Axes of the slice: x: 4, y: 8 (y_hi: 2, y_lo: 4; y = y_hi * 4 + y_lo), z: 8, core: 2. Of those that a mesh axis runs over, the one named last changes fastest.
Arguments:
- tokens: bfloat16 [8192, 2560], P(('dp', 'expert')), may hold values from -6 to 6
- grad_out: bfloat16 [8192, 2560], P(('dp', 'expert')), may hold values from -6 to 6
- expert_ids: int32 [8192, 2], P(('dp', 'expert')), may hold values from 0 to 63, as said below
- gates: bfloat16 [8192, 2], P(('dp', 'expert')), may hold values from 0.099609375 to 1
- w_gate: bfloat16 [64, 2560, 1024], P('expert', None, 'dp'), may hold values from -0.125 to 0.125
- w_up: bfloat16 [64, 2560, 1024], P('expert', None, 'dp'), may hold values from -0.125 to 0.125
- w_down: bfloat16 [64, 1024, 2560], P('expert', 'dp'), may hold values from -0.1875 to 0.1875
Outputs:
- out_tokens: bfloat16 [8192, 2560], P(('dp', 'expert'))
- grad_tokens: bfloat16 [8192, 2560], P(('dp', 'expert'))
- grad_gate: bfloat16 [64, 2560, 1024], P('expert', None, 'dp')
- grad_up: bfloat16 [64, 2560, 1024], P('expert', None, 'dp')
- grad_down: bfloat16 [64, 1024, 2560], P('expert', 'dp')
The draws below stay inside these ranges and needn't reach their ends.
Inputs may be any that keep to these rules, and one draw needn't show every extreme that they name: `expert_ids`: each token names 2 different experts. Over the tokens of all devices at one index of expert taken together, one expert, the same at every index, is named exactly 8 times; a second one, also the same at every index, exactly 5 times; every other expert at most 5 times.
All inputs are finite; a program needn't handle non-finite values.
Results may differ from the reference program's by a relative error of at most 0.019.
Values may be sent and summed in bfloat16 or wider, within the bound.
No kernel may reach another device: no remote copies, remote signals or barrier semaphores. Data moves between devices by JAX's collectives and lax.ppermute only.
A program may use at most 128 MiB of HBM per device.

```python
import math
import jax
import jax.numpy as jnp
from jax import lax

D = 2560
F = 1024
TOPK = 2
TOK_DEV = 16
EXPERTS = 64
F_DEV = 128
TOKENS = 8192
CAP_HOT = 8
CAP_LO = 5
N_DP = 8
N_EXPERT = 64


def draw_expert_ids(key, part):
    dp_count = TOKENS // (TOK_DEV * EXPERTS)
    group_rows = dp_count * TOK_DEV
    slots = group_rows * TOPK
    cold_count = EXPERTS - 2
    rest = slots - CAP_HOT - CAP_LO
    level = rest // cold_count
    extra = rest % cold_count
    spread = max(0, min(level, CAP_LO - level - 1))
    first_key, group_key = jax.random.split(jax.random.fold_in(key, 11))
    labels = jax.random.permutation(first_key, EXPERTS).astype(jnp.int32)

    def one_group(sub_key):
        shift_key, order_key, row_key = jax.random.split(sub_key, 3)
        base = level + (jnp.arange(cold_count) < extra).astype(jnp.int32)
        shifts = jax.random.randint(shift_key, (cold_count // 2,), -spread, spread + 1, dtype=jnp.int32)
        paired = jnp.stack([shifts, -shifts], axis=1).reshape(-1)
        paired = jnp.concatenate([paired, jnp.zeros((cold_count % 2,), jnp.int32)])
        cold = (base + paired)[jax.random.permutation(order_key, cold_count)]
        counts = jnp.concatenate([jnp.array([CAP_HOT, CAP_LO], jnp.int32), cold.astype(jnp.int32)])
        sequence = jnp.repeat(labels, counts, total_repeat_length=slots)
        table = sequence.reshape(TOPK, group_rows).T
        table = table[jax.random.permutation(row_key, group_rows)]
        return table.reshape(dp_count, TOK_DEV, TOPK)
    groups = jax.vmap(one_group)(jax.random.split(group_key, EXPERTS))
    return jnp.transpose(groups, (1, 0, 2, 3)).reshape(TOKENS, TOPK).astype(jnp.int32)


def level_of(stream_key, extent, cuts, least, high):
    gain, own = 1.0, jax.random.fold_in(stream_key, 6)
    for axis_at, shards_of in cuts:
        heights = jnp.exp(jax.random.uniform(jax.random.fold_in(own, axis_at), (shards_of,), jnp.float32, least / len(cuts), high / len(cuts)))
        gain = gain * jnp.repeat(heights, extent[axis_at] // shards_of).reshape([-1 if axis == axis_at else 1 for axis in range(len(extent))])
    return gain


def normal_values(rng, dims, deviation, most, cuts=(), held_as=jnp.bfloat16):
    entries = deviation * jax.random.normal(rng, dims, jnp.float32)
    if cuts:
        entries = entries * level_of(rng, dims, cuts, -0.22, 0.18)
    return jnp.clip(entries, -most, most).astype(held_as)


def setup_inputs(seed: int = 0) -> dict:
    key_list = jax.random.split(jax.random.key(seed), 8)
    tokens = normal_values(key_list[0], (TOKENS, D), 1.0, 6.0, ((0, 512),))
    grad_out = normal_values(key_list[1], (TOKENS, D), 1.0, 6.0, ((0, 512),))
    expert_ids = draw_expert_ids(jax.random.fold_in(key_list[7], 71), 0)
    gates = jnp.clip(jnp.exp(math.log(1.0) - 2.306499 * jax.random.uniform(key_list[3], (TOKENS, TOPK), jnp.float32) ** level_of(key_list[3], (TOKENS, TOPK), ((0, 512),), -0.2, 0.2)), 0.099609375, 1.0).astype(jnp.bfloat16)
    w_gate = normal_values(key_list[4], (EXPERTS, D, F), D ** -0.5, 0.125, ((0, 64), (2, 8)))
    w_up = normal_values(key_list[5], (EXPERTS, D, F), D ** -0.5, 0.125, ((0, 64), (2, 8)))
    w_down = normal_values(key_list[6], (EXPERTS, F, D), F ** -0.5, 0.1875, ((0, 64), (1, 8)))
    return dict(tokens=tokens, grad_out=grad_out, expert_ids=expert_ids, gates=gates, w_gate=w_gate, w_up=w_up, w_down=w_down)


def expert_math(rows_in, cot_in, gate_weight, up_weight, down_weight):
    gate_pre = jnp.dot(rows_in, gate_weight, preferred_element_type=jnp.float32)
    up_pre = jnp.dot(rows_in, up_weight, preferred_element_type=jnp.float32)
    hidden = (jax.nn.silu(gate_pre) * up_pre).astype(jnp.bfloat16)
    count = hidden.shape[0]
    hidden_blocks = hidden.astype(jnp.float32).reshape(count, N_DP, F_DEV)
    down_blocks = down_weight.astype(jnp.float32).reshape(N_DP, F_DEV, D)
    partial_value = jnp.einsum("rif,ifd->rid", hidden_blocks, down_blocks).astype(jnp.bfloat16)
    output = jnp.sum(partial_value.astype(jnp.float32), axis=1)
    grad_down = jnp.dot(hidden.T, cot_in, preferred_element_type=jnp.float32)
    d_hidden = jnp.dot(cot_in, down_weight.T, preferred_element_type=jnp.float32)
    sig = jax.nn.sigmoid(gate_pre)
    d_gate = (d_hidden * up_pre * sig * (1.0 + gate_pre * (1.0 - sig))).astype(jnp.bfloat16)
    d_up = (d_hidden * gate_pre * sig).astype(jnp.bfloat16)
    grad_gate = jnp.dot(rows_in.T, d_gate, preferred_element_type=jnp.float32)
    grad_up = jnp.dot(rows_in.T, d_up, preferred_element_type=jnp.float32)
    gate_blocks = gate_weight.astype(jnp.float32).reshape(D, N_DP, F_DEV)
    up_blocks = up_weight.astype(jnp.float32).reshape(D, N_DP, F_DEV)
    back = jnp.einsum("rif,dif->rid", d_gate.astype(jnp.float32).reshape(count, N_DP, F_DEV), gate_blocks)
    back = back + jnp.einsum("rif,dif->rid", d_up.astype(jnp.float32).reshape(count, N_DP, F_DEV), up_blocks)
    back_sum = jnp.sum(back.astype(jnp.bfloat16).astype(jnp.float32), axis=1)
    return output, back_sum, grad_gate, grad_up, grad_down


def reference(tokens, grad_out, expert_ids, gates, w_gate, w_up, w_down):
    flat_ids = expert_ids.reshape(-1).astype(jnp.int32)
    assigned = flat_ids.shape[0]
    token_of = (jnp.arange(assigned, dtype=jnp.int32) // TOPK).astype(jnp.int32)
    gate_flat = gates.reshape(-1).astype(jnp.float32)
    order = jnp.argsort(flat_ids, stable=True).astype(jnp.int32)
    counts = jnp.sum((flat_ids[:, None] == jnp.arange(EXPERTS, dtype=jnp.int32)[None, :]).astype(jnp.int32), axis=0)
    starts = (jnp.cumsum(counts) - counts).astype(jnp.int32)
    most = CAP_HOT * N_EXPERT
    padded = jnp.concatenate([order, jnp.zeros((most,), jnp.int32)])

    def one_expert(carry, inputs):
        out_total, back_total = carry
        expert, gate_weight, up_weight, down_weight = inputs
        picks = lax.dynamic_slice(padded, (starts[expert].astype(jnp.int32),), (most,))
        valid = jnp.arange(most, dtype=jnp.int32) < counts[expert]
        picks = jnp.where(valid, picks, 0).astype(jnp.int32)
        rows = token_of[picks]
        rows_in = jnp.where(valid[:, None], tokens[rows], jnp.zeros((), tokens.dtype))
        chosen = jnp.where(valid, gate_flat[picks], jnp.zeros((), gate_flat.dtype))
        cot_in = (chosen[:, None] * grad_out[rows].astype(jnp.float32)).astype(jnp.bfloat16)
        output, back_sum, grad_gate, grad_up, grad_down = expert_math(rows_in, cot_in, gate_weight, up_weight, down_weight)
        out_total = out_total.at[rows].add(chosen[:, None] * output)
        back_total = back_total.at[rows].add(jnp.where(valid[:, None], back_sum, jnp.zeros((), back_sum.dtype)))
        return (out_total, back_total), (grad_gate.astype(jnp.bfloat16), grad_up.astype(jnp.bfloat16), grad_down.astype(jnp.bfloat16))

    start = (jnp.zeros(tokens.shape, jnp.float32), jnp.zeros(tokens.shape, jnp.float32))
    (out_total, back_total), grads = lax.scan(one_expert, start, (jnp.arange(EXPERTS, dtype=jnp.int32), w_gate, w_up, w_down))
    return (out_total.astype(jnp.bfloat16), back_total.astype(jnp.bfloat16), grads[0], grads[1], grads[2])
```

```python
import jax
import jax.numpy as jnp
from jax import lax
from jax.sharding import PartitionSpec as P


def expert_rows(rows_in, cot_in, gate_weight, up_weight, down_weight):
    gate_pre = jnp.dot(rows_in, gate_weight, preferred_element_type=jnp.float32)
    up_pre = jnp.dot(rows_in, up_weight, preferred_element_type=jnp.float32)
    hidden = (jax.nn.silu(gate_pre) * up_pre).astype(jnp.bfloat16)
    partial_value = jnp.dot(hidden, down_weight, preferred_element_type=jnp.float32).astype(
        jnp.bfloat16
    )
    first_dim = (((0,), (0,)), ((), ()))
    last_dim = (((1,), (1,)), ((), ()))
    grad_down = lax.dot_general(hidden, cot_in, first_dim, preferred_element_type=jnp.float32)
    d_hidden = lax.dot_general(cot_in, down_weight, last_dim, preferred_element_type=jnp.float32)
    sig = jax.nn.sigmoid(gate_pre)
    d_gate = (d_hidden * up_pre * sig * (1.0 + gate_pre * (1.0 - sig))).astype(jnp.bfloat16)
    d_up = (d_hidden * gate_pre * sig).astype(jnp.bfloat16)
    grad_gate = lax.dot_general(rows_in, d_gate, first_dim, preferred_element_type=jnp.float32)
    grad_up = lax.dot_general(rows_in, d_up, first_dim, preferred_element_type=jnp.float32)
    back_term = lax.dot_general(d_gate, gate_weight, last_dim, preferred_element_type=jnp.float32)
    back_term = (
        back_term + lax.dot_general(d_up, up_weight, last_dim, preferred_element_type=jnp.float32)
    ).astype(jnp.bfloat16)
    return (partial_value, back_term, grad_gate, grad_up, grad_down)


def collect_slots(values, slot_index, weights):
    taken = jnp.take(values, slot_index.reshape(-1), axis=0, mode="fill", fill_value=0)
    taken = taken.reshape(slot_index.shape[0], slot_index.shape[1], values.shape[1]).astype(
        jnp.float32
    )
    if weights is None:
        return jnp.sum(taken, axis=1)
    return jnp.sum(weights.astype(jnp.float32)[:, :, None] * taken, axis=1)


def body(tokens, grad_out, expert_ids, gates, w_gate, w_up, w_down):
    dp_count = lax.axis_size("dp")
    experts = lax.axis_size("expert")
    local_rows = tokens.shape[0]
    width = tokens.shape[1]
    top_count = expert_ids.shape[1]
    group_rows = dp_count * local_rows
    assigned = group_rows * top_count
    mean_slots = assigned // experts
    cap_hot = 2 * mean_slots
    side = 128
    extra = jnp.concatenate(
        [
            expert_ids.astype(jnp.bfloat16),
            gates,
            jnp.zeros((local_rows, side - 2 * top_count), jnp.bfloat16),
        ],
        axis=1,
    )
    packed = jnp.concatenate([tokens, grad_out, extra], axis=1)
    group = lax.all_gather(packed, "dp", axis=0, tiled=True)
    group_tokens = group[:, :width]
    group_grads = group[:, width : 2 * width]
    group_ids = group[:, 2 * width : 2 * width + top_count].astype(jnp.int32)
    group_gates = group[:, 2 * width + top_count : 2 * width + 2 * top_count]

    flat_ids = group_ids.reshape(-1)
    expert_range = jnp.arange(experts, dtype=jnp.int32)
    member = (flat_ids[:, None] == expert_range[None, :]).astype(jnp.int32)
    before = jnp.sum((jnp.cumsum(member, axis=0) - member) * member, axis=1)
    slot_count = experts * cap_hot
    slot_of = (flat_ids * cap_hot + before).astype(jnp.int32)

    owner = jnp.full((slot_count,), assigned, jnp.int32)
    owner = owner.at[slot_of].set(jnp.arange(assigned, dtype=jnp.int32), mode="drop")
    filled = owner < assigned
    safe = jnp.where(filled, owner, 0)
    tok = safe // top_count
    gate_of = jnp.where(filled, group_gates.reshape(-1)[safe].astype(jnp.float32), 0.0)
    rows_taken = jnp.where(filled[:, None], group_tokens[tok], jnp.zeros((), jnp.bfloat16))
    cot_taken = (gate_of[:, None] * group_grads[tok].astype(jnp.float32)).astype(jnp.bfloat16)
    send = jnp.concatenate([rows_taken, cot_taken], axis=1)
    arrived = lax.all_to_all(
        send.reshape(experts, cap_hot, 2 * width), "expert", 0, 0, tiled=True
    ).reshape(slot_count, 2 * width)

    partial_value, back_term, grad_gate, grad_up, grad_down = expert_rows(
        arrived[:, :width],
        arrived[:, width:],
        w_gate[0],
        w_up[0],
        w_down[0],
    )
    ret = jnp.concatenate([partial_value, back_term], axis=1)
    returned = lax.all_to_all(
        ret.reshape(experts, cap_hot, 2 * width), "expert", 0, 0, tiled=True
    ).reshape(slot_count, 2 * width)
    slot_pairs = slot_of.reshape(group_rows, top_count)
    out_part = collect_slots(returned[:, :width], slot_pairs, group_gates)
    back_part = collect_slots(returned[:, width:], slot_pairs, None)
    both = jnp.concatenate([out_part, back_part], axis=1).astype(jnp.bfloat16)
    spread = lax.all_to_all(
        both.reshape(dp_count, local_rows, 2 * width), "dp", 0, 0, tiled=True
    )
    total = jnp.sum(spread.astype(jnp.float32), axis=0).astype(jnp.bfloat16)
    return (
        total[:, :width],
        total[:, width:],
        grad_gate.astype(jnp.bfloat16)[None],
        grad_up.astype(jnp.bfloat16)[None],
        grad_down.astype(jnp.bfloat16)[None],
    )


def solution(mesh):
    in_specs = (
        P(("dp", "expert"), None),
        P(("dp", "expert"), None),
        P(("dp", "expert"), None),
        P(("dp", "expert"), None),
        P("expert", None, "dp"),
        P("expert", None, "dp"),
        P("expert", "dp", None),
    )
    out_specs = (
        P(("dp", "expert"), None),
        P(("dp", "expert"), None),
        P("expert", None, "dp"),
        P("expert", None, "dp"),
        P("expert", "dp", None),
    )
    return jax.shard_map(body, mesh=mesh, in_specs=in_specs, out_specs=out_specs, check_vma=False)
```

```python
import jax
import jax.numpy as jnp
from jax import lax
from jax.sharding import PartitionSpec as P


def expert_rows(rows_in, cot_in, gate_weight, up_weight, down_weight):
    gate_pre = jnp.dot(rows_in, gate_weight, preferred_element_type=jnp.float32)
    up_pre = jnp.dot(rows_in, up_weight, preferred_element_type=jnp.float32)
    hidden = (jax.nn.silu(gate_pre) * up_pre).astype(jnp.bfloat16)
    partial_value = jnp.dot(hidden, down_weight, preferred_element_type=jnp.float32).astype(
        jnp.bfloat16
    )
    first_dim = (((0,), (0,)), ((), ()))
    last_dim = (((1,), (1,)), ((), ()))
    grad_down = lax.dot_general(hidden, cot_in, first_dim, preferred_element_type=jnp.float32)
    d_hidden = lax.dot_general(cot_in, down_weight, last_dim, preferred_element_type=jnp.float32)
    sig = jax.nn.sigmoid(gate_pre)
    d_gate = (d_hidden * up_pre * sig * (1.0 + gate_pre * (1.0 - sig))).astype(jnp.bfloat16)
    d_up = (d_hidden * gate_pre * sig).astype(jnp.bfloat16)
    grad_gate = lax.dot_general(rows_in, d_gate, first_dim, preferred_element_type=jnp.float32)
    grad_up = lax.dot_general(rows_in, d_up, first_dim, preferred_element_type=jnp.float32)
    back_term = lax.dot_general(d_gate, gate_weight, last_dim, preferred_element_type=jnp.float32)
    back_term = (
        back_term + lax.dot_general(d_up, up_weight, last_dim, preferred_element_type=jnp.float32)
    ).astype(jnp.bfloat16)
    return (partial_value, back_term, grad_gate, grad_up, grad_down)


def body(tokens, grad_out, expert_ids, gates, w_gate, w_up, w_down):
    dp_count = lax.axis_size("dp")
    experts = lax.axis_size("expert")
    local_rows = tokens.shape[0]
    width = tokens.shape[1]
    top_count = expert_ids.shape[1]
    group_rows = dp_count * local_rows
    assigned = group_rows * top_count
    mean_slots = assigned // experts
    cap_hot = 2 * mean_slots
    side = 128
    extra = jnp.concatenate(
        [
            expert_ids.astype(jnp.bfloat16),
            gates,
            jnp.zeros((local_rows, side - 2 * top_count), jnp.bfloat16),
        ],
        axis=1,
    )
    packed = jnp.concatenate([tokens, grad_out, extra], axis=1)
    copies = jnp.broadcast_to(packed[None], (dp_count,) + packed.shape)
    group = lax.all_to_all(copies, "dp", 0, 0, tiled=True).reshape(group_rows, packed.shape[1])
    group_tokens = group[:, :width]
    group_grads = group[:, width : 2 * width]
    group_ids = group[:, 2 * width : 2 * width + top_count].astype(jnp.int32)
    group_gates = group[:, 2 * width + top_count : 2 * width + 2 * top_count]

    flat_ids = group_ids.reshape(-1)
    expert_range = jnp.arange(experts, dtype=jnp.int32)
    member = (flat_ids[:, None] == expert_range[None, :]).astype(jnp.int32)
    before = jnp.sum((jnp.cumsum(member, axis=0) - member) * member, axis=1)
    slot_count = experts * cap_hot
    slot_pairs = (flat_ids * cap_hot + before).astype(jnp.int32).reshape(group_rows, top_count)
    slot_range = jnp.arange(slot_count, dtype=jnp.int32)[:, None]
    pick = jnp.zeros((slot_count, group_rows), jnp.bfloat16)
    weigh = jnp.zeros((slot_count, group_rows), jnp.bfloat16)
    for k in range(top_count):
        hit = slot_pairs[:, k][None, :] == slot_range
        pick = jnp.where(hit, jnp.ones((), jnp.bfloat16), pick)
        weigh = jnp.where(hit, group_gates[:, k][None, :], weigh)
    rows_taken = jnp.dot(pick, group_tokens, preferred_element_type=jnp.float32).astype(jnp.bfloat16)
    cot_taken = jnp.dot(weigh, group_grads, preferred_element_type=jnp.float32).astype(jnp.bfloat16)
    send = jnp.concatenate([rows_taken, cot_taken], axis=1)
    arrived = lax.all_to_all(
        send.reshape(experts, cap_hot, 2 * width), "expert", 0, 0, tiled=True
    ).reshape(slot_count, 2 * width)

    partial_value, back_term, grad_gate, grad_up, grad_down = expert_rows(
        arrived[:, :width],
        arrived[:, width:],
        w_gate[0],
        w_up[0],
        w_down[0],
    )
    ret = jnp.concatenate([partial_value, back_term], axis=1)
    returned = lax.all_to_all(
        ret.reshape(experts, cap_hot, 2 * width), "expert", 0, 0, tiled=True
    ).reshape(slot_count, 2 * width)
    first_dim = (((0,), (0,)), ((), ()))
    out_part = lax.dot_general(
        weigh, returned[:, :width], first_dim, preferred_element_type=jnp.float32
    )
    back_part = lax.dot_general(
        pick, returned[:, width:], first_dim, preferred_element_type=jnp.float32
    )
    both = jnp.concatenate([out_part, back_part], axis=1).astype(jnp.bfloat16)
    spread = lax.all_to_all(
        both.reshape(dp_count, local_rows, 2 * width), "dp", 0, 0, tiled=True
    )
    total = jnp.sum(spread.astype(jnp.float32), axis=0).astype(jnp.bfloat16)
    return (
        total[:, :width],
        total[:, width:],
        grad_gate.astype(jnp.bfloat16)[None],
        grad_up.astype(jnp.bfloat16)[None],
        grad_down.astype(jnp.bfloat16)[None],
    )


def solution(mesh):
    in_specs = (
        P(("dp", "expert"), None),
        P(("dp", "expert"), None),
        P(("dp", "expert"), None),
        P(("dp", "expert"), None),
        P("expert", None, "dp"),
        P("expert", None, "dp"),
        P("expert", "dp", None),
    )
    out_specs = (
        P(("dp", "expert"), None),
        P(("dp", "expert"), None),
        P("expert", None, "dp"),
        P("expert", None, "dp"),
        P("expert", "dp", None),
    )
    return jax.shard_map(body, mesh=mesh, in_specs=in_specs, out_specs=out_specs, check_vma=False)
```

```python
import jax
import jax.numpy as jnp
from jax import lax
from jax.sharding import PartitionSpec as P


def dp_gather(block, dp_count):
    copies = jnp.broadcast_to(block[None], (dp_count,) + block.shape)
    gathered = lax.all_to_all(copies, "dp", 0, 0, tiled=True)
    return gathered.reshape(dp_count * block.shape[0], block.shape[1])


def expert_swap(block, experts, cap):
    shaped = block.reshape(experts, cap, block.shape[1])
    return lax.all_to_all(shaped, "expert", 0, 0, tiled=True).reshape(block.shape)


def dp_sum(part, dp_count, local_rows):
    spread = lax.all_to_all(
        part.astype(jnp.bfloat16).reshape(dp_count, local_rows, part.shape[1]), "dp", 0, 0, tiled=True
    )
    return jnp.sum(spread.astype(jnp.float32), axis=0).astype(jnp.bfloat16)


def body(tokens, grad_out, expert_ids, gates, w_gate, w_up, w_down):
    dp_count = lax.axis_size("dp")
    experts = lax.axis_size("expert")
    local_rows = tokens.shape[0]
    width = tokens.shape[1]
    top_count = expert_ids.shape[1]
    group_rows = dp_count * local_rows
    assigned = group_rows * top_count
    mean_slots = assigned // experts
    cap_hot = 2 * mean_slots
    side = 128
    extra = jnp.concatenate(
        [
            expert_ids.astype(jnp.bfloat16),
            gates,
            jnp.zeros((local_rows, side - 2 * top_count), jnp.bfloat16),
        ],
        axis=1,
    )
    group = dp_gather(jnp.concatenate([tokens, extra], axis=1), dp_count)
    group_grads = dp_gather(grad_out, dp_count)
    group_tokens = group[:, :width]
    group_ids = group[:, width : width + top_count].astype(jnp.int32)
    group_gates = group[:, width + top_count : width + 2 * top_count]

    flat_ids = group_ids.reshape(-1)
    expert_range = jnp.arange(experts, dtype=jnp.int32)
    member = (flat_ids[:, None] == expert_range[None, :]).astype(jnp.int32)
    before = jnp.sum((jnp.cumsum(member, axis=0) - member) * member, axis=1)
    slot_count = experts * cap_hot
    slot_pairs = (flat_ids * cap_hot + before).astype(jnp.int32).reshape(group_rows, top_count)
    slot_range = jnp.arange(slot_count, dtype=jnp.int32)[:, None]
    pick = jnp.zeros((slot_count, group_rows), jnp.bfloat16)
    weigh = jnp.zeros((slot_count, group_rows), jnp.bfloat16)
    for k in range(top_count):
        hit = slot_pairs[:, k][None, :] == slot_range
        pick = jnp.where(hit, jnp.ones((), jnp.bfloat16), pick)
        weigh = jnp.where(hit, group_gates[:, k][None, :], weigh)
    first_dim = (((0,), (0,)), ((), ()))
    last_dim = (((1,), (1,)), ((), ()))

    rows_taken = jnp.dot(pick, group_tokens, preferred_element_type=jnp.float32).astype(jnp.bfloat16)
    rows_in = expert_swap(rows_taken, experts, cap_hot)
    gate_weight, up_weight, down_weight = w_gate[0], w_up[0], w_down[0]
    gate_pre = jnp.dot(rows_in, gate_weight, preferred_element_type=jnp.float32)
    up_pre = jnp.dot(rows_in, up_weight, preferred_element_type=jnp.float32)
    hidden = (jax.nn.silu(gate_pre) * up_pre).astype(jnp.bfloat16)
    partial_value = jnp.dot(hidden, down_weight, preferred_element_type=jnp.float32).astype(
        jnp.bfloat16
    )
    partial_back = expert_swap(partial_value, experts, cap_hot)
    out_part = lax.dot_general(weigh, partial_back, first_dim, preferred_element_type=jnp.float32)
    out_sum = dp_sum(out_part, dp_count, local_rows)

    cot_taken = jnp.dot(weigh, group_grads, preferred_element_type=jnp.float32).astype(jnp.bfloat16)
    cot_in = expert_swap(cot_taken, experts, cap_hot)
    d_hidden = lax.dot_general(cot_in, down_weight, last_dim, preferred_element_type=jnp.float32)
    sig = jax.nn.sigmoid(gate_pre)
    d_gate = (d_hidden * up_pre * sig * (1.0 + gate_pre * (1.0 - sig))).astype(jnp.bfloat16)
    d_up = (d_hidden * gate_pre * sig).astype(jnp.bfloat16)
    back_term = lax.dot_general(d_gate, gate_weight, last_dim, preferred_element_type=jnp.float32)
    back_term = (
        back_term + lax.dot_general(d_up, up_weight, last_dim, preferred_element_type=jnp.float32)
    ).astype(jnp.bfloat16)
    back_ret = expert_swap(back_term, experts, cap_hot)
    back_part = lax.dot_general(pick, back_ret, first_dim, preferred_element_type=jnp.float32)
    back_sum = dp_sum(back_part, dp_count, local_rows)

    grad_down = lax.dot_general(hidden, cot_in, first_dim, preferred_element_type=jnp.float32)
    grad_gate = lax.dot_general(rows_in, d_gate, first_dim, preferred_element_type=jnp.float32)
    grad_up = lax.dot_general(rows_in, d_up, first_dim, preferred_element_type=jnp.float32)
    return (
        out_sum,
        back_sum,
        grad_gate.astype(jnp.bfloat16)[None],
        grad_up.astype(jnp.bfloat16)[None],
        grad_down.astype(jnp.bfloat16)[None],
    )


def solution(mesh):
    in_specs = (
        P(("dp", "expert"), None),
        P(("dp", "expert"), None),
        P(("dp", "expert"), None),
        P(("dp", "expert"), None),
        P("expert", None, "dp"),
        P("expert", None, "dp"),
        P("expert", "dp", None),
    )
    out_specs = (
        P(("dp", "expert"), None),
        P(("dp", "expert"), None),
        P("expert", None, "dp"),
        P("expert", None, "dp"),
        P("expert", "dp", None),
    )
    return jax.shard_map(body, mesh=mesh, in_specs=in_specs, out_specs=out_specs, check_vma=False)
```

```python
import jax
import jax.numpy as jnp
from jax import lax
from jax.experimental import pallas as pl
from jax.experimental.pallas import tpu as pltpu
from jax.sharding import PartitionSpec as P


def expert_kernel(rows_ref, cot_ref, gate_ref, up_ref, down_ref, part_ref, back_ref, hid_ref, dg_ref, du_ref):
    last_dim = (((1,), (1,)), ((), ()))
    rows_in = rows_ref[...]
    gate_pre = jnp.dot(rows_in, gate_ref[...], preferred_element_type=jnp.float32)
    up_pre = jnp.dot(rows_in, up_ref[...], preferred_element_type=jnp.float32)
    sig = 1.0 / (1.0 + jnp.exp(-gate_pre))
    hidden = (gate_pre * sig * up_pre).astype(jnp.bfloat16)
    hid_ref[...] = hidden
    part_ref[...] = jnp.dot(hidden, down_ref[...], preferred_element_type=jnp.float32).astype(
        jnp.bfloat16
    )
    d_hidden = lax.dot_general(
        cot_ref[...], down_ref[...], last_dim, preferred_element_type=jnp.float32
    )
    d_gate = (d_hidden * up_pre * sig * (1.0 + gate_pre * (1.0 - sig))).astype(jnp.bfloat16)
    d_up = (d_hidden * gate_pre * sig).astype(jnp.bfloat16)
    dg_ref[...] = d_gate
    du_ref[...] = d_up
    back = lax.dot_general(d_gate, gate_ref[...], last_dim, preferred_element_type=jnp.float32)
    back = back + lax.dot_general(d_up, up_ref[...], last_dim, preferred_element_type=jnp.float32)
    back_ref[...] = back.astype(jnp.bfloat16)


def expert_rows(rows_in, cot_in, gate_weight, up_weight, down_weight):
    count, width = rows_in.shape
    hidden_width = gate_weight.shape[1]
    wide = jax.ShapeDtypeStruct((count, width), jnp.bfloat16)
    narrow = jax.ShapeDtypeStruct((count, hidden_width), jnp.bfloat16)
    partial_value, back_term, hidden, d_gate, d_up = pl.pallas_call(
        expert_kernel,
        out_shape=(wide, wide, narrow, narrow, narrow),
        compiler_params=pltpu.CompilerParams(vmem_limit_bytes=48 * 1024 * 1024),
    )(rows_in, cot_in, gate_weight, up_weight, down_weight)
    first_dim = (((0,), (0,)), ((), ()))
    grad_down = lax.dot_general(hidden, cot_in, first_dim, preferred_element_type=jnp.float32)
    grad_gate = lax.dot_general(rows_in, d_gate, first_dim, preferred_element_type=jnp.float32)
    grad_up = lax.dot_general(rows_in, d_up, first_dim, preferred_element_type=jnp.float32)
    return (partial_value, back_term, grad_gate, grad_up, grad_down)


def body(tokens, grad_out, expert_ids, gates, w_gate, w_up, w_down):
    dp_count = lax.axis_size("dp")
    experts = lax.axis_size("expert")
    local_rows = tokens.shape[0]
    width = tokens.shape[1]
    top_count = expert_ids.shape[1]
    group_rows = dp_count * local_rows
    assigned = group_rows * top_count
    mean_slots = assigned // experts
    cap_hot = 2 * mean_slots
    side = 128
    extra = jnp.concatenate(
        [
            expert_ids.astype(jnp.bfloat16),
            gates,
            jnp.zeros((local_rows, side - 2 * top_count), jnp.bfloat16),
        ],
        axis=1,
    )
    packed = jnp.concatenate([tokens, grad_out, extra], axis=1)
    copies = jnp.broadcast_to(packed[None], (dp_count,) + packed.shape)
    group = lax.all_to_all(copies, "dp", 0, 0, tiled=True).reshape(group_rows, packed.shape[1])
    group_tokens = group[:, :width]
    group_grads = group[:, width : 2 * width]
    group_ids = group[:, 2 * width : 2 * width + top_count].astype(jnp.int32)
    group_gates = group[:, 2 * width + top_count : 2 * width + 2 * top_count]

    flat_ids = group_ids.reshape(-1)
    expert_range = jnp.arange(experts, dtype=jnp.int32)
    member = (flat_ids[:, None] == expert_range[None, :]).astype(jnp.int32)
    before = jnp.sum((jnp.cumsum(member, axis=0) - member) * member, axis=1)
    slot_count = experts * cap_hot
    slot_pairs = (flat_ids * cap_hot + before).astype(jnp.int32).reshape(group_rows, top_count)
    slot_range = jnp.arange(slot_count, dtype=jnp.int32)[:, None]
    pick = jnp.zeros((slot_count, group_rows), jnp.bfloat16)
    weigh = jnp.zeros((slot_count, group_rows), jnp.bfloat16)
    for k in range(top_count):
        hit = slot_pairs[:, k][None, :] == slot_range
        pick = jnp.where(hit, jnp.ones((), jnp.bfloat16), pick)
        weigh = jnp.where(hit, group_gates[:, k][None, :], weigh)
    rows_taken = jnp.dot(pick, group_tokens, preferred_element_type=jnp.float32).astype(jnp.bfloat16)
    cot_taken = jnp.dot(weigh, group_grads, preferred_element_type=jnp.float32).astype(jnp.bfloat16)
    send = jnp.concatenate([rows_taken, cot_taken], axis=1)
    arrived = lax.all_to_all(
        send.reshape(experts, cap_hot, 2 * width), "expert", 0, 0, tiled=True
    ).reshape(slot_count, 2 * width)

    partial_value, back_term, grad_gate, grad_up, grad_down = expert_rows(
        arrived[:, :width],
        arrived[:, width:],
        w_gate[0],
        w_up[0],
        w_down[0],
    )
    ret = jnp.concatenate([partial_value, back_term], axis=1)
    returned = lax.all_to_all(
        ret.reshape(experts, cap_hot, 2 * width), "expert", 0, 0, tiled=True
    ).reshape(slot_count, 2 * width)
    first_dim = (((0,), (0,)), ((), ()))
    out_part = lax.dot_general(
        weigh, returned[:, :width], first_dim, preferred_element_type=jnp.float32
    )
    back_part = lax.dot_general(
        pick, returned[:, width:], first_dim, preferred_element_type=jnp.float32
    )
    both = jnp.concatenate([out_part, back_part], axis=1).astype(jnp.bfloat16)
    spread = lax.all_to_all(
        both.reshape(dp_count, local_rows, 2 * width), "dp", 0, 0, tiled=True
    )
    total = jnp.sum(spread.astype(jnp.float32), axis=0).astype(jnp.bfloat16)
    return (
        total[:, :width],
        total[:, width:],
        grad_gate.astype(jnp.bfloat16)[None],
        grad_up.astype(jnp.bfloat16)[None],
        grad_down.astype(jnp.bfloat16)[None],
    )


def solution(mesh):
    in_specs = (
        P(("dp", "expert"), None),
        P(("dp", "expert"), None),
        P(("dp", "expert"), None),
        P(("dp", "expert"), None),
        P("expert", None, "dp"),
        P("expert", None, "dp"),
        P("expert", "dp", None),
    )
    out_specs = (
        P(("dp", "expert"), None),
        P(("dp", "expert"), None),
        P("expert", None, "dp"),
        P("expert", None, "dp"),
        P("expert", "dp", None),
    )
    return jax.shard_map(body, mesh=mesh, in_specs=in_specs, out_specs=out_specs, check_vma=False)
```

```python
import jax
import jax.numpy as jnp
from jax import lax
from jax.sharding import PartitionSpec as P


def expert_rows(rows_in, cot_in, gate_weight, up_weight, down_weight):
    hidden_width = gate_weight.shape[1]
    both_weight = jnp.concatenate([gate_weight, up_weight], axis=1)
    both_pre = jnp.dot(rows_in, both_weight, preferred_element_type=jnp.float32)
    gate_pre = both_pre[:, :hidden_width]
    up_pre = both_pre[:, hidden_width:]
    hidden = (jax.nn.silu(gate_pre) * up_pre).astype(jnp.bfloat16)
    partial_value = jnp.dot(hidden, down_weight, preferred_element_type=jnp.float32).astype(
        jnp.bfloat16
    )
    first_dim = (((0,), (0,)), ((), ()))
    last_dim = (((1,), (1,)), ((), ()))
    grad_down = lax.dot_general(hidden, cot_in, first_dim, preferred_element_type=jnp.float32)
    d_hidden = lax.dot_general(cot_in, down_weight, last_dim, preferred_element_type=jnp.float32)
    sig = jax.nn.sigmoid(gate_pre)
    d_gate = (d_hidden * up_pre * sig * (1.0 + gate_pre * (1.0 - sig))).astype(jnp.bfloat16)
    d_up = (d_hidden * gate_pre * sig).astype(jnp.bfloat16)
    grad_gate = lax.dot_general(rows_in, d_gate, first_dim, preferred_element_type=jnp.float32)
    grad_up = lax.dot_general(rows_in, d_up, first_dim, preferred_element_type=jnp.float32)
    d_both = jnp.concatenate([d_gate, d_up], axis=1)
    back_term = lax.dot_general(
        d_both, both_weight, last_dim, preferred_element_type=jnp.float32
    ).astype(jnp.bfloat16)
    return (partial_value, back_term, grad_gate, grad_up, grad_down)


def body(tokens, grad_out, expert_ids, gates, w_gate, w_up, w_down):
    dp_count = lax.axis_size("dp")
    experts = lax.axis_size("expert")
    local_rows = tokens.shape[0]
    width = tokens.shape[1]
    top_count = expert_ids.shape[1]
    group_rows = dp_count * local_rows
    assigned = group_rows * top_count
    mean_slots = assigned // experts
    cap_hot = 2 * mean_slots
    side = 128
    extra = jnp.concatenate(
        [
            expert_ids.astype(jnp.bfloat16),
            gates,
            jnp.zeros((local_rows, side - 2 * top_count), jnp.bfloat16),
        ],
        axis=1,
    )
    packed = jnp.concatenate([tokens, grad_out, extra], axis=1)
    copies = jnp.broadcast_to(packed[None], (dp_count,) + packed.shape)
    group = lax.all_to_all(copies, "dp", 0, 0, tiled=True).reshape(group_rows, packed.shape[1])
    group_tokens = group[:, :width]
    group_grads = group[:, width : 2 * width]
    group_ids = group[:, 2 * width : 2 * width + top_count].astype(jnp.int32)
    group_gates = group[:, 2 * width + top_count : 2 * width + 2 * top_count]

    flat_ids = group_ids.reshape(-1)
    expert_range = jnp.arange(experts, dtype=jnp.int32)
    member = (flat_ids[:, None] == expert_range[None, :]).astype(jnp.int32)
    before = jnp.sum((jnp.cumsum(member, axis=0) - member) * member, axis=1)
    slot_count = experts * cap_hot
    slot_pairs = (flat_ids * cap_hot + before).astype(jnp.int32).reshape(group_rows, top_count)
    slot_range = jnp.arange(slot_count, dtype=jnp.int32)[:, None]
    pick = jnp.zeros((slot_count, group_rows), jnp.bfloat16)
    weigh = jnp.zeros((slot_count, group_rows), jnp.bfloat16)
    for k in range(top_count):
        hit = slot_pairs[:, k][None, :] == slot_range
        pick = jnp.where(hit, jnp.ones((), jnp.bfloat16), pick)
        weigh = jnp.where(hit, group_gates[:, k][None, :], weigh)
    rows_taken = jnp.dot(pick, group_tokens, preferred_element_type=jnp.float32).astype(jnp.bfloat16)
    cot_taken = jnp.dot(weigh, group_grads, preferred_element_type=jnp.float32).astype(jnp.bfloat16)
    send = jnp.concatenate([rows_taken, cot_taken], axis=1)
    arrived = lax.all_to_all(
        send.reshape(experts, cap_hot, 2 * width), "expert", 0, 0, tiled=True
    ).reshape(slot_count, 2 * width)

    partial_value, back_term, grad_gate, grad_up, grad_down = expert_rows(
        arrived[:, :width],
        arrived[:, width:],
        w_gate[0],
        w_up[0],
        w_down[0],
    )
    ret = jnp.concatenate([partial_value, back_term], axis=1)
    returned = lax.all_to_all(
        ret.reshape(experts, cap_hot, 2 * width), "expert", 0, 0, tiled=True
    ).reshape(slot_count, 2 * width)
    first_dim = (((0,), (0,)), ((), ()))
    out_part = lax.dot_general(
        weigh, returned[:, :width], first_dim, preferred_element_type=jnp.float32
    )
    back_part = lax.dot_general(
        pick, returned[:, width:], first_dim, preferred_element_type=jnp.float32
    )
    both = jnp.concatenate([out_part, back_part], axis=1).astype(jnp.bfloat16)
    spread = lax.all_to_all(
        both.reshape(dp_count, local_rows, 2 * width), "dp", 0, 0, tiled=True
    )
    total = jnp.sum(spread.astype(jnp.float32), axis=0).astype(jnp.bfloat16)
    return (
        total[:, :width],
        total[:, width:],
        grad_gate.astype(jnp.bfloat16)[None],
        grad_up.astype(jnp.bfloat16)[None],
        grad_down.astype(jnp.bfloat16)[None],
    )


def solution(mesh):
    in_specs = (
        P(("dp", "expert"), None),
        P(("dp", "expert"), None),
        P(("dp", "expert"), None),
        P(("dp", "expert"), None),
        P("expert", None, "dp"),
        P("expert", None, "dp"),
        P("expert", "dp", None),
    )
    out_specs = (
        P(("dp", "expert"), None),
        P(("dp", "expert"), None),
        P("expert", None, "dp"),
        P("expert", None, "dp"),
        P("expert", "dp", None),
    )
    return jax.shard_map(body, mesh=mesh, in_specs=in_specs, out_specs=out_specs, check_vma=False)
```

```python
import jax
import jax.numpy as jnp
from jax import lax
from jax.sharding import PartitionSpec as P


def expert_rows(rows_in, cot_in, gate_weight, up_weight, down_weight):
    hidden_width = gate_weight.shape[1]
    both_weight = jnp.concatenate([gate_weight, up_weight], axis=1)
    both_pre = jnp.dot(rows_in, both_weight, preferred_element_type=jnp.float32)
    gate_pre = both_pre[:, :hidden_width]
    up_pre = both_pre[:, hidden_width:]
    hidden = (jax.nn.silu(gate_pre) * up_pre).astype(jnp.bfloat16)
    partial_value = jnp.dot(hidden, down_weight, preferred_element_type=jnp.float32).astype(
        jnp.bfloat16
    )
    first_dim = (((0,), (0,)), ((), ()))
    last_dim = (((1,), (1,)), ((), ()))
    grad_down = lax.dot_general(hidden, cot_in, first_dim, preferred_element_type=jnp.float32)
    d_hidden = lax.dot_general(cot_in, down_weight, last_dim, preferred_element_type=jnp.float32)
    sig = jax.nn.sigmoid(gate_pre)
    d_gate = (d_hidden * up_pre * sig * (1.0 + gate_pre * (1.0 - sig))).astype(jnp.bfloat16)
    d_up = (d_hidden * gate_pre * sig).astype(jnp.bfloat16)
    grad_gate = lax.dot_general(rows_in, d_gate, first_dim, preferred_element_type=jnp.float32)
    grad_up = lax.dot_general(rows_in, d_up, first_dim, preferred_element_type=jnp.float32)
    d_both = jnp.concatenate([d_gate, d_up], axis=1)
    back_term = lax.dot_general(
        d_both, both_weight, last_dim, preferred_element_type=jnp.float32
    ).astype(jnp.bfloat16)
    return (partial_value, back_term, grad_gate, grad_up, grad_down)


def body(tokens, grad_out, expert_ids, gates, w_gate, w_up, w_down):
    dp_count = lax.axis_size("dp")
    experts = lax.axis_size("expert")
    local_rows = tokens.shape[0]
    width = tokens.shape[1]
    top_count = expert_ids.shape[1]
    group_rows = dp_count * local_rows
    assigned = group_rows * top_count
    mean_slots = assigned // experts
    cap_hot = 2 * mean_slots
    side = 128
    extra = jnp.concatenate(
        [
            expert_ids.astype(jnp.bfloat16),
            gates,
            jnp.zeros((local_rows, side - 2 * top_count), jnp.bfloat16),
        ],
        axis=1,
    )
    packed = jnp.concatenate([tokens, grad_out, extra], axis=1)
    copies = jnp.broadcast_to(packed[None], (dp_count,) + packed.shape)
    group = lax.all_to_all(copies, "dp", 0, 0, tiled=True).reshape(group_rows, packed.shape[1])
    group_tokens = group[:, :width]
    group_grads = group[:, width : 2 * width]
    group_ids = group[:, 2 * width : 2 * width + top_count].astype(jnp.int32)
    group_gates = group[:, 2 * width + top_count : 2 * width + 2 * top_count]

    flat_ids = group_ids.reshape(-1)
    expert_range = jnp.arange(experts, dtype=jnp.int32)
    member = (flat_ids[:, None] == expert_range[None, :]).astype(jnp.bfloat16)
    route_range = jnp.arange(assigned, dtype=jnp.int32)
    earlier = (route_range[None, :] < route_range[:, None]).astype(jnp.bfloat16)
    prefix = jnp.dot(earlier, member, preferred_element_type=jnp.float32)
    before = jnp.sum(prefix * member.astype(jnp.float32), axis=1).astype(jnp.int32)
    slot_count = experts * cap_hot
    slot_pairs = (flat_ids * cap_hot + before).astype(jnp.int32).reshape(group_rows, top_count)
    slot_range = jnp.arange(slot_count, dtype=jnp.int32)[:, None]
    pick = jnp.zeros((slot_count, group_rows), jnp.bfloat16)
    weigh = jnp.zeros((slot_count, group_rows), jnp.bfloat16)
    for k in range(top_count):
        hit = slot_pairs[:, k][None, :] == slot_range
        pick = jnp.where(hit, jnp.ones((), jnp.bfloat16), pick)
        weigh = jnp.where(hit, group_gates[:, k][None, :], weigh)
    rows_taken = jnp.dot(pick, group_tokens, preferred_element_type=jnp.float32).astype(jnp.bfloat16)
    cot_taken = jnp.dot(weigh, group_grads, preferred_element_type=jnp.float32).astype(jnp.bfloat16)
    send = jnp.concatenate([rows_taken, cot_taken], axis=1)
    arrived = lax.all_to_all(
        send.reshape(experts, cap_hot, 2 * width), "expert", 0, 0, tiled=True
    ).reshape(slot_count, 2 * width)

    partial_value, back_term, grad_gate, grad_up, grad_down = expert_rows(
        arrived[:, :width],
        arrived[:, width:],
        w_gate[0],
        w_up[0],
        w_down[0],
    )
    ret = jnp.concatenate([partial_value, back_term], axis=1)
    returned = lax.all_to_all(
        ret.reshape(experts, cap_hot, 2 * width), "expert", 0, 0, tiled=True
    ).reshape(slot_count, 2 * width)
    first_dim = (((0,), (0,)), ((), ()))
    out_part = lax.dot_general(
        weigh, returned[:, :width], first_dim, preferred_element_type=jnp.float32
    )
    back_part = lax.dot_general(
        pick, returned[:, width:], first_dim, preferred_element_type=jnp.float32
    )
    both = jnp.concatenate([out_part, back_part], axis=1).astype(jnp.bfloat16)
    spread = lax.all_to_all(
        both.reshape(dp_count, local_rows, 2 * width), "dp", 0, 0, tiled=True
    )
    total = jnp.sum(spread.astype(jnp.float32), axis=0).astype(jnp.bfloat16)
    return (
        total[:, :width],
        total[:, width:],
        grad_gate.astype(jnp.bfloat16)[None],
        grad_up.astype(jnp.bfloat16)[None],
        grad_down.astype(jnp.bfloat16)[None],
    )


def solution(mesh):
    in_specs = (
        P(("dp", "expert"), None),
        P(("dp", "expert"), None),
        P(("dp", "expert"), None),
        P(("dp", "expert"), None),
        P("expert", None, "dp"),
        P("expert", None, "dp"),
        P("expert", "dp", None),
    )
    out_specs = (
        P(("dp", "expert"), None),
        P(("dp", "expert"), None),
        P("expert", None, "dp"),
        P("expert", None, "dp"),
        P("expert", "dp", None),
    )
    return jax.shard_map(body, mesh=mesh, in_specs=in_specs, out_specs=out_specs, check_vma=False)
```
